1024 devices in a mesh: wave: 64 (over x, y_lo, core), lev: 16 (over z, y_hi).
Axes of the slice: x: 8, y: 8 (y_hi: 2, y_lo: 4; y = y_hi * 4 + y_lo), z: 8, core: 2. Of those that a mesh axis runs over, the one named last changes fastest.
Arguments:
- spectrum: bfloat16 [16, 4, 320, 768], P('lev', None, 'wave'), may hold values from -0.25 to 0.25
- legendre: bfloat16 [320, 640, 768], P('wave'), may hold values from -0.3125 to 0.3125
- owners: int32 [640], replicated, may hold values from 0 to 639, as said below
Outputs:
- spectral_tend: float32 [16, 4, 320, 768], P('lev', None, 'wave')
The draws below stay inside these ranges and needn't reach their ends.
Inputs may be any that keep to these rules, and one draw needn't show every extreme that they name: `owners`: every wavenumber appears in exactly one slot, and slots 2p and 2p+1 hold two wavenumbers that add up to 639.
All inputs are finite; a program needn't handle non-finite values.
Results may differ from the reference program's by a relative error of at most 0.0059.
Values may be sent and summed in bfloat16 or wider, within the bound.
No kernel may reach another device: no remote copies, remote signals or barrier semaphores. Data moves between devices by JAX's collectives and lax.ppermute only.
A program may use at most 32 MiB of HBM per device.

```python
import math
import jax
import jax.numpy as jnp
from jax import lax

M = 640
NLAT = 1280
LON = 2688
NLATH = 640
PAIRS = 320
NPK = 768
LEVELS = 16
N_WAVE = 64


def draw_owners(key, part):
    order_key = jax.random.fold_in(key, 11)
    flip_key = jax.random.fold_in(key, 12)
    smaller = jax.random.permutation(order_key, jnp.arange(PAIRS, dtype=jnp.int32))
    flip_bits = jax.random.randint(flip_key, (PAIRS,), 0, 2, dtype=jnp.int32)
    leading = jnp.where(flip_bits == 1, M - 1 - smaller, smaller)
    return jnp.stack([leading, M - 1 - leading], axis=1).reshape(M).astype(jnp.int32)


def block_scale(key, extent, cuts, least, top_value):
    gain, own = 1.0, jax.random.fold_in(key, 6)
    for axis_at, shards_of in cuts:
        steps = jnp.exp(jax.random.uniform(jax.random.fold_in(own, axis_at), (shards_of,), jnp.float32, least / len(cuts), top_value / len(cuts)))
        gain = gain * jnp.repeat(steps, extent[axis_at] // shards_of).reshape([-1 if axis == axis_at else 1 for axis in range(len(extent))])
    return gain


def scatter_about(key, extent, deviation, reach, shards=(), kind=jnp.bfloat16):
    loudness = block_scale(key, extent, shards, -0.22, 0.18) if shards else 1.0
    result = jax.random.normal(key, extent, jnp.float32) * deviation * loudness
    return jnp.minimum(jnp.maximum(result, -reach), reach).astype(kind)


def setup_inputs(seed: int = 0) -> dict:
    key_list = jax.random.split(jax.random.key(seed), 4)
    spectrum = scatter_about(key_list[0], (LEVELS, 4, PAIRS, NPK), M ** -0.5, 0.25, ((0, 16), (2, 64)))
    legendre = scatter_about(key_list[1], (PAIRS, NLATH, NPK), (M // 2) ** -0.5, 0.3125, ((0, 64),))
    owners = draw_owners(jax.random.fold_in(key_list[3], 71), 0)
    return {"spectrum": spectrum, "legendre": legendre, "owners": owners}


def pair_masks(leading):
    packed = jnp.arange(NPK, dtype=jnp.int32)[None, :]
    split_at = (M - leading)[:, None]
    in_first = (packed < split_at).astype(jnp.float32)
    in_second = ((packed >= split_at) & (packed < M + 1)).astype(jnp.float32)
    sign_first = (1 - 2 * (packed % 2)).astype(jnp.float32)
    sign_second = (1 - 2 * ((packed - split_at) % 2)).astype(jnp.float32)
    return (in_first, in_second, sign_first, sign_second)

def make_table(owners, lon_count):
    columns = jnp.arange(lon_count, dtype=jnp.int32)
    phases = owners[:, None] * columns[None, :] % lon_count
    angles = phases.astype(jnp.float32) * (2.0 * math.pi / lon_count)
    return jnp.concatenate([jnp.cos(angles), -jnp.sin(angles)], axis=0).astype(jnp.bfloat16)

def synthesize(coeffs, wave_table):
    row_block = coeffs.reshape(-1, wave_table.shape[0])
    grid_vals = jnp.dot(row_block, wave_table, preferred_element_type=jnp.float32)
    return grid_vals.reshape(coeffs.shape[0], coeffs.shape[1], 2, wave_table.shape[1])

def advect(padded):
    centre = padded[:, 1:-1]
    slopes = 0.5 * (padded[:, 2:] - padded[:, :-2])
    leading = centre[:, :, 0] * slopes[:, :, 1]
    second = centre[:, :, 1] * slopes[:, :, 0] + 0.5 * centre[:, :, 0] * centre[:, :, 1]
    return jnp.stack([leading, second], axis=2).astype(jnp.bfloat16)

def analyze(tendency, wave_table, lat_start):
    row_block = tendency.reshape(-1, tendency.shape[-1])
    result_rows = lax.dot_general(row_block, wave_table, (((1,), (1,)), ((), ())), preferred_element_type=jnp.float32)
    latitude = lat_start + jnp.arange(tendency.shape[0], dtype=jnp.int32)
    weight = jnp.sin((latitude.astype(jnp.float32) + 0.5) * (math.pi / NLAT)) / math.sqrt(NLAT)
    result_rows = result_rows.reshape(tendency.shape[0], -1) * weight[:, None]
    return result_rows.astype(jnp.bfloat16).reshape(tendency.shape[0], tendency.shape[1], 4, wave_table.shape[0] // 2)

def reference(spectrum, legendre, owners):
    in_first, in_second, sign_first, sign_second = pair_masks(owners[0::2])
    spec_rows = spectrum.astype(jnp.float32).reshape(LEVELS * 4, PAIRS, NPK)
    masked = jnp.stack([spec_rows * in_first, spec_rows * in_second, spec_rows * in_first * sign_first, spec_rows * in_second * sign_second], axis=2)

    def inverse_pair(inputs):
        pair_part, table_rows = inputs
        return jnp.einsum('cvk,jk->jcv', pair_part, table_rows.astype(jnp.float32))
    waves = lax.map(inverse_pair, (jnp.moveaxis(masked, 1, 0), legendre)).astype(jnp.bfloat16)
    northern = jnp.transpose(waves[..., :2], (1, 2, 0, 3)).reshape(NLATH, LEVELS, 4, M)
    southern = jnp.transpose(waves[..., 2:], (1, 2, 0, 3)).reshape(NLATH, LEVELS, 4, M)[::-1]
    fourier = jnp.concatenate([northern, southern], axis=0)
    wave_table = make_table(owners, LON)
    lat_band = NLAT // N_WAVE
    blocks = fourier.reshape(N_WAVE, lat_band, LEVELS, 4, M)
    starts = jnp.arange(N_WAVE, dtype=jnp.int32) * lat_band

    def grid_block(inputs):
        coeffs, lat_start = inputs
        grid_vals = synthesize(coeffs, wave_table)
        padded = jnp.pad(grid_vals, ((0, 0), (1, 1), (0, 0), (0, 0)))
        return analyze(advect(padded), wave_table, lat_start)
    banded = lax.map(grid_block, (blocks, starts)).reshape(NLAT, LEVELS, 4, M)
    northern = banded[:NLATH].reshape(NLATH, LEVELS * 4, PAIRS, 2)
    southern = banded[NLATH:][::-1].reshape(NLATH, LEVELS * 4, PAIRS, 2)
    halves = jnp.concatenate([northern, southern], axis=3)

    def direct_pair(inputs):
        pair_part, table_rows = inputs
        return jnp.einsum('jcv,jk->cvk', pair_part.astype(jnp.float32), table_rows.astype(jnp.float32))
    partial_value = lax.map(direct_pair, (jnp.moveaxis(halves, 2, 0), legendre))
    tendency_sum = in_first[:, None, :] * (partial_value[:, :, 0] + sign_first[:, None, :] * partial_value[:, :, 2]) + in_second[:, None, :] * (partial_value[:, :, 1] + sign_second[:, None, :] * partial_value[:, :, 3])
    return jnp.transpose(tendency_sum, (1, 0, 2)).reshape(LEVELS, 4, PAIRS, NPK)
```

```python
import math

import jax
import jax.numpy as jnp
from jax import lax
from jax.sharding import PartitionSpec as P

M = 640
NLAT = 1280
LON = 2688
NLATH = 640
NPK = 768


def with_halo(block, sides, width):
    for axis, dim in sides:
        count = lax.axis_size(axis)
        forward = [(i, i + 1) for i in range(count - 1)]
        backward = [(target, source) for source, target in forward]
        low = lax.ppermute(
            lax.slice_in_dim(block, block.shape[dim] - width, None, axis=dim), axis, forward
        )
        high = lax.ppermute(lax.slice_in_dim(block, 0, width, axis=dim), axis, backward)
        block = jnp.concatenate([low, block, high], axis=dim)
    return block


def pair_masks(leading):
    packed = jnp.arange(NPK, dtype=jnp.int32)[None, :]
    split_at = (M - leading)[:, None]
    in_first = (packed < split_at).astype(jnp.float32)
    in_second = ((packed >= split_at) & (packed < M + 1)).astype(jnp.float32)
    sign_first = (1 - 2 * (packed % 2)).astype(jnp.float32)
    sign_second = (1 - 2 * ((packed - split_at) % 2)).astype(jnp.float32)
    return (in_first, in_second, sign_first, sign_second)


def make_table(owners, lon_count):
    inner = 128 if lon_count % 128 == 0 else lon_count
    outer = lon_count // inner
    scale = 2.0 * math.pi / lon_count
    fine = jnp.arange(inner, dtype=jnp.int32)
    coarse = jnp.arange(outer, dtype=jnp.int32) * inner
    fine_angle = (owners[:, None] * fine[None, :] % lon_count).astype(jnp.float32) * scale
    coarse_angle = (owners[:, None] * coarse[None, :] % lon_count).astype(jnp.float32) * scale
    cos_f, sin_f = jnp.cos(fine_angle)[:, None, :], jnp.sin(fine_angle)[:, None, :]
    cos_c, sin_c = jnp.cos(coarse_angle)[:, :, None], jnp.sin(coarse_angle)[:, :, None]
    cos_t = (cos_c * cos_f - sin_c * sin_f).reshape(owners.shape[0], lon_count)
    sin_t = (sin_c * cos_f + cos_c * sin_f).reshape(owners.shape[0], lon_count)
    return jnp.concatenate([cos_t, -sin_t], axis=0).astype(jnp.bfloat16)


def synthesize(coeffs, wave_table):
    row_block = coeffs.reshape(-1, wave_table.shape[0])
    grid_vals = jnp.dot(row_block, wave_table, preferred_element_type=jnp.float32)
    return grid_vals.reshape(coeffs.shape[0], coeffs.shape[1], 2, wave_table.shape[1])


def advect(padded):
    centre = padded[:, 1:-1]
    slopes = 0.5 * (padded[:, 2:] - padded[:, :-2])
    leading = centre[:, :, 0] * slopes[:, :, 1]
    second = centre[:, :, 1] * slopes[:, :, 0] + 0.5 * centre[:, :, 0] * centre[:, :, 1]
    return jnp.stack([leading, second], axis=2).astype(jnp.bfloat16)


def analyze(tendency, wave_table, lat_start):
    row_block = tendency.reshape(-1, tendency.shape[-1])
    result_rows = lax.dot_general(
        row_block, wave_table, (((1,), (1,)), ((), ())), preferred_element_type=jnp.float32
    )
    latitude = lat_start + jnp.arange(tendency.shape[0], dtype=jnp.int32)
    weight = jnp.sin((latitude.astype(jnp.float32) + 0.5) * (math.pi / NLAT)) / math.sqrt(NLAT)
    result_rows = result_rows.reshape(tendency.shape[0], -1) * weight[:, None]
    return result_rows.astype(jnp.bfloat16).reshape(
        tendency.shape[0], tendency.shape[1], 4, wave_table.shape[0] // 2
    )


def shards(spectrum, legendre, owners):
    lev_count = spectrum.shape[0]
    pair_count = spectrum.shape[2]
    slot_count = 2 * pair_count
    lat_band = NLAT // lax.axis_size("wave")
    pair_base = lax.axis_index("wave") * pair_count
    leading = lax.dynamic_slice_in_dim(owners[0::2], pair_base, pair_count)
    in_first, in_second, sign_first, sign_second = pair_masks(leading)
    mask_first = in_first.astype(jnp.bfloat16)
    mask_second = in_second.astype(jnp.bfloat16)
    signed_first = (in_first * sign_first).astype(jnp.bfloat16)
    signed_second = (in_second * sign_second).astype(jnp.bfloat16)
    spec_rows = spectrum.reshape(lev_count * 4, pair_count, NPK)
    masked = jnp.stack(
        [
            spec_rows * mask_first,
            spec_rows * mask_second,
            spec_rows * signed_first,
            spec_rows * signed_second,
        ],
        axis=2,
    )
    waves = jnp.einsum(
        "cpvk,pjk->jcpv", masked, legendre, preferred_element_type=jnp.float32
    ).astype(jnp.bfloat16)
    northern = waves[..., :2].reshape(NLATH, lev_count, 4, slot_count)
    southern = waves[..., 2:].reshape(NLATH, lev_count, 4, slot_count)[::-1]
    fourier = jnp.concatenate([northern, southern], axis=0)
    banded = lax.all_to_all(fourier, "wave", split_axis=0, concat_axis=3, tiled=True)
    wave_table = make_table(owners, LON)
    lat_start = lax.axis_index("wave") * lat_band
    padded = synthesize(with_halo(banded, (("lev", 1),), 1), wave_table)
    coeffs = analyze(advect(padded), wave_table, lat_start)
    owned_rows = lax.all_to_all(coeffs, "wave", split_axis=3, concat_axis=0, tiled=True)
    northern = owned_rows[:NLATH].reshape(NLATH, lev_count * 4, pair_count, 2)
    southern = owned_rows[NLATH:][::-1].reshape(NLATH, lev_count * 4, pair_count, 2)
    halves = jnp.concatenate([northern, southern], axis=3)
    partial_value = jnp.einsum(
        "jcpv,pjk->cpvk", halves, legendre, preferred_element_type=jnp.float32
    )
    tendency_sum = in_first * (
        partial_value[:, :, 0] + sign_first * partial_value[:, :, 2]
    ) + in_second * (partial_value[:, :, 1] + sign_second * partial_value[:, :, 3])
    return tendency_sum.reshape(lev_count, 4, pair_count, NPK)


def solution(mesh):
    in_specs = (P("lev", None, "wave", None), P("wave", None, None), P())
    out_specs = P("lev", None, "wave", None)
    return jax.shard_map(shards, mesh=mesh, in_specs=in_specs, out_specs=out_specs, check_vma=False)
```

```python
import math

import jax
import jax.numpy as jnp
from jax import lax
from jax.experimental import pallas as pl
from jax.sharding import PartitionSpec as P

M = 640
NLAT = 1280
LON = 2688
NLATH = 640
NPK = 768


def with_halo(block, sides, width):
    for axis, dim in sides:
        count = lax.axis_size(axis)
        forward = [(i, i + 1) for i in range(count - 1)]
        backward = [(target, source) for source, target in forward]
        low = lax.ppermute(
            lax.slice_in_dim(block, block.shape[dim] - width, None, axis=dim), axis, forward
        )
        high = lax.ppermute(lax.slice_in_dim(block, 0, width, axis=dim), axis, backward)
        block = jnp.concatenate([low, block, high], axis=dim)
    return block


def pair_masks(leading):
    packed = jnp.arange(NPK, dtype=jnp.int32)[None, :]
    split_at = (M - leading)[:, None]
    in_first = (packed < split_at).astype(jnp.float32)
    in_second = ((packed >= split_at) & (packed < M + 1)).astype(jnp.float32)
    sign_first = (1 - 2 * (packed % 2)).astype(jnp.float32)
    sign_second = (1 - 2 * ((packed - split_at) % 2)).astype(jnp.float32)
    return (in_first, in_second, sign_first, sign_second)


def table_kernel(cos_c_ref, sin_c_ref, cos_f_ref, sin_f_ref, out_ref):
    inner = cos_f_ref.shape[1]
    cos_f = cos_f_ref[...]
    sin_f = sin_f_ref[...]
    for k in range(cos_c_ref.shape[1]):
        cos_c = cos_c_ref[:, k : k + 1]
        sin_c = sin_c_ref[:, k : k + 1]
        columns = slice(k * inner, (k + 1) * inner)
        out_ref[0, :, columns] = (cos_c * cos_f - sin_c * sin_f).astype(out_ref.dtype)
        out_ref[1, :, columns] = (-(sin_c * cos_f + cos_c * sin_f)).astype(out_ref.dtype)


def make_table(owners, lon_count):
    inner = 128 if lon_count % 128 == 0 else lon_count
    outer = lon_count // inner
    scale = 2.0 * math.pi / lon_count
    fine = jnp.arange(inner, dtype=jnp.int32)
    coarse = jnp.arange(outer, dtype=jnp.int32) * inner
    fine_angle = (owners[:, None] * fine[None, :] % lon_count).astype(jnp.float32) * scale
    coarse_angle = (owners[:, None] * coarse[None, :] % lon_count).astype(jnp.float32) * scale
    rows = owners.shape[0]
    block = 128 if rows % 128 == 0 else rows
    table = pl.pallas_call(
        table_kernel,
        grid=(rows // block,),
        in_specs=[
            pl.BlockSpec((block, outer), lambda i: (i, 0)),
            pl.BlockSpec((block, outer), lambda i: (i, 0)),
            pl.BlockSpec((block, inner), lambda i: (i, 0)),
            pl.BlockSpec((block, inner), lambda i: (i, 0)),
        ],
        out_specs=pl.BlockSpec((2, block, lon_count), lambda i: (0, i, 0)),
        out_shape=jax.ShapeDtypeStruct((2, rows, lon_count), jnp.bfloat16),
    )(jnp.cos(coarse_angle), jnp.sin(coarse_angle), jnp.cos(fine_angle), jnp.sin(fine_angle))
    return table.reshape(2 * rows, lon_count)


def synthesize(coeffs, wave_table):
    row_block = coeffs.reshape(-1, wave_table.shape[0])
    grid_vals = jnp.dot(row_block, wave_table, preferred_element_type=jnp.float32)
    return grid_vals.reshape(coeffs.shape[0], coeffs.shape[1], 2, wave_table.shape[1])


def advect(padded):
    centre = padded[:, 1:-1]
    slopes = 0.5 * (padded[:, 2:] - padded[:, :-2])
    leading = centre[:, :, 0] * slopes[:, :, 1]
    second = centre[:, :, 1] * slopes[:, :, 0] + 0.5 * centre[:, :, 0] * centre[:, :, 1]
    return jnp.stack([leading, second], axis=2).astype(jnp.bfloat16)


def analyze(tendency, wave_table, lat_start):
    row_block = tendency.reshape(-1, tendency.shape[-1])
    result_rows = lax.dot_general(
        row_block, wave_table, (((1,), (1,)), ((), ())), preferred_element_type=jnp.float32
    )
    latitude = lat_start + jnp.arange(tendency.shape[0], dtype=jnp.int32)
    weight = jnp.sin((latitude.astype(jnp.float32) + 0.5) * (math.pi / NLAT)) / math.sqrt(NLAT)
    result_rows = result_rows.reshape(tendency.shape[0], -1) * weight[:, None]
    return result_rows.astype(jnp.bfloat16).reshape(
        tendency.shape[0], tendency.shape[1], 4, wave_table.shape[0] // 2
    )


def shards(spectrum, legendre, owners):
    lev_count = spectrum.shape[0]
    pair_count = spectrum.shape[2]
    slot_count = 2 * pair_count
    lat_band = NLAT // lax.axis_size("wave")
    pair_base = lax.axis_index("wave") * pair_count
    leading = lax.dynamic_slice_in_dim(owners[0::2], pair_base, pair_count)
    in_first, in_second, sign_first, sign_second = pair_masks(leading)
    mask_first = in_first.astype(jnp.bfloat16)
    mask_second = in_second.astype(jnp.bfloat16)
    signed_first = (in_first * sign_first).astype(jnp.bfloat16)
    signed_second = (in_second * sign_second).astype(jnp.bfloat16)
    spec_rows = spectrum.reshape(lev_count * 4, pair_count, NPK)
    masked = jnp.stack(
        [
            spec_rows * mask_first,
            spec_rows * mask_second,
            spec_rows * signed_first,
            spec_rows * signed_second,
        ],
        axis=2,
    )
    waves = jnp.einsum(
        "cpvk,pjk->jcpv", masked, legendre, preferred_element_type=jnp.float32
    ).astype(jnp.bfloat16)
    northern = waves[..., :2].reshape(NLATH, lev_count, 4, slot_count)
    southern = waves[..., 2:].reshape(NLATH, lev_count, 4, slot_count)[::-1]
    fourier = jnp.concatenate([northern, southern], axis=0)
    banded = lax.all_to_all(fourier, "wave", split_axis=0, concat_axis=3, tiled=True)
    wave_table = make_table(owners, LON)
    lat_start = lax.axis_index("wave") * lat_band
    padded = synthesize(with_halo(banded, (("lev", 1),), 1), wave_table)
    coeffs = analyze(advect(padded), wave_table, lat_start)
    owned_rows = lax.all_to_all(coeffs, "wave", split_axis=3, concat_axis=0, tiled=True)
    northern = owned_rows[:NLATH].reshape(NLATH, lev_count * 4, pair_count, 2)
    southern = owned_rows[NLATH:][::-1].reshape(NLATH, lev_count * 4, pair_count, 2)
    halves = jnp.concatenate([northern, southern], axis=3)
    partial_value = jnp.einsum(
        "jcpv,pjk->cpvk", halves, legendre, preferred_element_type=jnp.float32
    )
    tendency_sum = in_first * (
        partial_value[:, :, 0] + sign_first * partial_value[:, :, 2]
    ) + in_second * (partial_value[:, :, 1] + sign_second * partial_value[:, :, 3])
    return tendency_sum.reshape(lev_count, 4, pair_count, NPK)


def solution(mesh):
    in_specs = (P("lev", None, "wave", None), P("wave", None, None), P())
    out_specs = P("lev", None, "wave", None)
    return jax.shard_map(shards, mesh=mesh, in_specs=in_specs, out_specs=out_specs, check_vma=False)
```

```python
import math

import jax
import jax.numpy as jnp
from jax import lax
from jax.experimental import pallas as pl
from jax.sharding import PartitionSpec as P

M = 640
NLAT = 1280
LON = 2688
NLATH = 640
NPK = 768


def with_halo(block, sides, width):
    for axis, dim in sides:
        count = lax.axis_size(axis)
        forward = [(i, i + 1) for i in range(count - 1)]
        backward = [(target, source) for source, target in forward]
        low = lax.ppermute(
            lax.slice_in_dim(block, block.shape[dim] - width, None, axis=dim), axis, forward
        )
        high = lax.ppermute(lax.slice_in_dim(block, 0, width, axis=dim), axis, backward)
        block = jnp.concatenate([low, block, high], axis=dim)
    return block


def pair_masks(leading):
    packed = jnp.arange(NPK, dtype=jnp.int32)[None, :]
    split_at = (M - leading)[:, None]
    in_first = (packed < split_at).astype(jnp.float32)
    in_second = ((packed >= split_at) & (packed < M + 1)).astype(jnp.float32)
    sign_first = (1 - 2 * (packed % 2)).astype(jnp.float32)
    sign_second = (1 - 2 * ((packed - split_at) % 2)).astype(jnp.float32)
    return (in_first, in_second, sign_first, sign_second)


def table_kernel(cos_c_ref, sin_c_ref, cos_f_ref, sin_f_ref, out_ref):
    inner = cos_f_ref.shape[1]
    cos_f = cos_f_ref[...]
    sin_f = sin_f_ref[...]
    for k in range(cos_c_ref.shape[1]):
        cos_c = cos_c_ref[:, k : k + 1]
        sin_c = sin_c_ref[:, k : k + 1]
        out_ref[:, k * inner : (k + 1) * inner] = (cos_c * cos_f - sin_c * sin_f).astype(out_ref.dtype)


def make_table(row_wave, row_part, lon_count):
    inner = 128 if lon_count % 128 == 0 else lon_count
    outer = lon_count // inner
    scale = 2.0 * math.pi / lon_count
    fine = jnp.arange(inner, dtype=jnp.int32)
    coarse = jnp.arange(outer, dtype=jnp.int32) * inner
    fine_angle = (row_wave[:, None] * fine[None, :] % lon_count).astype(jnp.float32) * scale
    coarse_angle = (row_wave[:, None] * coarse[None, :] % lon_count).astype(jnp.float32) * scale
    is_cos = (row_part == 0)[:, None]
    cos_c, sin_c = jnp.cos(coarse_angle), jnp.sin(coarse_angle)
    lead_c = jnp.where(is_cos, cos_c, -sin_c)
    lead_s = jnp.where(is_cos, sin_c, cos_c)
    rows = row_wave.shape[0]
    block = 128 if rows % 128 == 0 else rows
    return pl.pallas_call(
        table_kernel,
        grid=(rows // block,),
        in_specs=[
            pl.BlockSpec((block, outer), lambda i: (i, 0)),
            pl.BlockSpec((block, outer), lambda i: (i, 0)),
            pl.BlockSpec((block, inner), lambda i: (i, 0)),
            pl.BlockSpec((block, inner), lambda i: (i, 0)),
        ],
        out_specs=pl.BlockSpec((block, lon_count), lambda i: (i, 0)),
        out_shape=jax.ShapeDtypeStruct((rows, lon_count), jnp.bfloat16),
    )(lead_c, lead_s, jnp.cos(fine_angle), jnp.sin(fine_angle))


def shards(spectrum, legendre, owners):
    lev_count = spectrum.shape[0]
    pair_count = spectrum.shape[2]
    slot_count = 2 * pair_count
    wave_count = lax.axis_size("wave")
    lat_count = NLATH // wave_count
    wave_index = lax.axis_index("wave")
    pair_base = wave_index * pair_count
    leading = lax.dynamic_slice_in_dim(owners[0::2], pair_base, pair_count)
    in_first, in_second, sign_first, sign_second = pair_masks(leading)
    mask_first = in_first.astype(jnp.bfloat16)
    mask_second = in_second.astype(jnp.bfloat16)
    signed_first = (in_first * sign_first).astype(jnp.bfloat16)
    signed_second = (in_second * sign_second).astype(jnp.bfloat16)
    spec_rows = spectrum.reshape(lev_count * 4, pair_count, NPK)
    masked = jnp.stack(
        [
            spec_rows * mask_first,
            spec_rows * mask_second,
            spec_rows * signed_first,
            spec_rows * signed_second,
        ],
        axis=2,
    ).reshape(lev_count, 2, 2, pair_count, 2, 2, NPK)
    leg_blocks = legendre.reshape(pair_count, wave_count, lat_count, NPK)
    payload = jnp.einsum(
        "lfrphqk,pwjk->wrpqlhjf", masked, leg_blocks, preferred_element_type=jnp.float32
    ).astype(jnp.bfloat16)
    local_k = 2 * slot_count
    row_count = lev_count * 2 * lat_count * 2
    payload = payload.reshape(wave_count, local_k, row_count)
    received = lax.all_to_all(payload, "wave", 0, 0, tiled=True)
    row_wave = jnp.broadcast_to(
        owners.reshape(wave_count, 1, slot_count), (wave_count, 2, slot_count)
    ).reshape(-1)
    row_part = jnp.broadcast_to(
        jnp.arange(2, dtype=jnp.int32)[None, :, None], (wave_count, 2, slot_count)
    ).reshape(-1)
    wave_table = make_table(row_wave, row_part, LON)
    k_all = wave_count * local_k
    fourier = received.reshape(k_all, lev_count, 2 * lat_count * 2)
    fourier = with_halo(fourier, (("lev", 1),), 1).reshape(k_all, -1)
    grid_vals = lax.dot_general(
        fourier, wave_table, (((0,), (0,)), ((), ())), preferred_element_type=jnp.float32
    ).reshape(lev_count + 2, 2, lat_count, 2, LON)
    centre = grid_vals[1:-1]
    slopes = 0.5 * (grid_vals[2:] - grid_vals[:-2])
    lead_t = centre[:, :, :, 0] * slopes[:, :, :, 1]
    second_t = centre[:, :, :, 1] * slopes[:, :, :, 0] + 0.5 * centre[:, :, :, 0] * centre[:, :, :, 1]
    tendency = jnp.stack([lead_t, second_t], axis=3).astype(jnp.bfloat16).reshape(row_count, LON)
    north = wave_index * lat_count + jnp.arange(lat_count, dtype=jnp.int32)
    latitude = jnp.stack([north, NLAT - 1 - north], axis=0)
    weight = jnp.sin((latitude.astype(jnp.float32) + 0.5) * (math.pi / NLAT)) / math.sqrt(NLAT)
    weight = jnp.broadcast_to(weight[None, :, :, None], (lev_count, 2, lat_count, 2)).reshape(-1)
    coeffs = lax.dot_general(
        wave_table, tendency, (((1,), (1,)), ((), ())), preferred_element_type=jnp.float32
    )
    coeffs = (coeffs * weight[None, :]).astype(jnp.bfloat16)
    owned = lax.all_to_all(coeffs.reshape(wave_count, local_k, row_count), "wave", 0, 0, tiled=True)
    owned = owned.reshape(wave_count, 2, pair_count, 2, lev_count, 2, lat_count, 2)
    partial = jnp.einsum(
        "wrpqlhjf,pwjk->lfrpqhk", owned, leg_blocks, preferred_element_type=jnp.float32
    )
    tendency_sum = in_first * (
        partial[:, :, :, :, 0, 0] + sign_first * partial[:, :, :, :, 0, 1]
    ) + in_second * (partial[:, :, :, :, 1, 0] + sign_second * partial[:, :, :, :, 1, 1])
    return tendency_sum.reshape(lev_count, 4, pair_count, NPK)


def solution(mesh):
    in_specs = (P("lev", None, "wave", None), P("wave", None, None), P())
    out_specs = P("lev", None, "wave", None)
    return jax.shard_map(shards, mesh=mesh, in_specs=in_specs, out_specs=out_specs, check_vma=False)
```

```python
import math

import jax
import jax.numpy as jnp
from jax import lax
from jax.experimental import pallas as pl
from jax.sharding import PartitionSpec as P

M = 640
NLAT = 1280
LON = 2688
NLATH = 640
NPK = 768


def with_halo(block, sides, width):
    for axis, dim in sides:
        count = lax.axis_size(axis)
        forward = [(i, i + 1) for i in range(count - 1)]
        backward = [(target, source) for source, target in forward]
        low = lax.ppermute(
            lax.slice_in_dim(block, block.shape[dim] - width, None, axis=dim), axis, forward
        )
        high = lax.ppermute(lax.slice_in_dim(block, 0, width, axis=dim), axis, backward)
        block = jnp.concatenate([low, block, high], axis=dim)
    return block


def pair_masks(leading):
    packed = jnp.arange(NPK, dtype=jnp.int32)[None, :]
    split_at = (M - leading)[:, None]
    in_first = (packed < split_at).astype(jnp.float32)
    in_second = ((packed >= split_at) & (packed < M + 1)).astype(jnp.float32)
    sign_first = (1 - 2 * (packed % 2)).astype(jnp.float32)
    sign_second = (1 - 2 * ((packed - split_at) % 2)).astype(jnp.float32)
    return (in_first, in_second, sign_first, sign_second)


def table_kernel(cos_c_ref, sin_c_ref, cos_f_ref, sin_f_ref, out_ref):
    inner = cos_f_ref.shape[1]
    cos_f = cos_f_ref[...]
    sin_f = sin_f_ref[...]
    for k in range(cos_c_ref.shape[1]):
        cos_c = cos_c_ref[:, k : k + 1]
        sin_c = sin_c_ref[:, k : k + 1]
        columns = slice(k * inner, (k + 1) * inner)
        out_ref[0, :, columns] = (cos_c * cos_f - sin_c * sin_f).astype(out_ref.dtype)
        out_ref[1, :, columns] = (-(sin_c * cos_f + cos_c * sin_f)).astype(out_ref.dtype)


def make_table(owners, lon_count):
    inner = 128 if lon_count % 128 == 0 else lon_count
    outer = lon_count // inner
    scale = 2.0 * math.pi / lon_count
    fine = jnp.arange(inner, dtype=jnp.int32)
    coarse = jnp.arange(outer, dtype=jnp.int32) * inner
    fine_angle = (owners[:, None] * fine[None, :] % lon_count).astype(jnp.float32) * scale
    coarse_angle = (owners[:, None] * coarse[None, :] % lon_count).astype(jnp.float32) * scale
    rows = owners.shape[0]
    block = 128 if rows % 128 == 0 else rows
    table = pl.pallas_call(
        table_kernel,
        grid=(rows // block,),
        in_specs=[
            pl.BlockSpec((block, outer), lambda i: (i, 0)),
            pl.BlockSpec((block, outer), lambda i: (i, 0)),
            pl.BlockSpec((block, inner), lambda i: (i, 0)),
            pl.BlockSpec((block, inner), lambda i: (i, 0)),
        ],
        out_specs=pl.BlockSpec((2, block, lon_count), lambda i: (0, i, 0)),
        out_shape=jax.ShapeDtypeStruct((2, rows, lon_count), jnp.bfloat16),
    )(jnp.cos(coarse_angle), jnp.sin(coarse_angle), jnp.cos(fine_angle), jnp.sin(fine_angle))
    return table.reshape(2 * rows, lon_count)


def shards(spectrum, legendre, owners):
    lev_count = spectrum.shape[0]
    pair_count = spectrum.shape[2]
    slot_count = 2 * pair_count
    wave_count = lax.axis_size("wave")
    lat_count = NLATH // wave_count
    wave_index = lax.axis_index("wave")
    pair_base = wave_index * pair_count
    leading = lax.dynamic_slice_in_dim(owners[0::2], pair_base, pair_count)
    in_first, in_second, sign_first, sign_second = pair_masks(leading)
    mask_first = in_first.astype(jnp.bfloat16)
    mask_second = in_second.astype(jnp.bfloat16)
    signed_first = (in_first * sign_first).astype(jnp.bfloat16)
    signed_second = (in_second * sign_second).astype(jnp.bfloat16)
    spec_rows = spectrum.reshape(lev_count * 4, pair_count, NPK)
    masked = jnp.stack(
        [
            spec_rows * mask_first,
            spec_rows * mask_second,
            spec_rows * signed_first,
            spec_rows * signed_second,
        ],
        axis=2,
    ).reshape(lev_count, 2, 2, pair_count, 2, 2, NPK)
    waves = jnp.einsum(
        "lfrphqk,pjk->jrpqlhf", masked, legendre, preferred_element_type=jnp.float32
    ).astype(jnp.bfloat16)
    waves = waves.reshape(wave_count, lat_count, 2, pair_count, 2, lev_count, 2, 2)
    payload = jnp.transpose(waves, (0, 2, 3, 4, 5, 6, 1, 7))
    local_k = 2 * slot_count
    row_count = lev_count * 2 * lat_count * 2
    payload = payload.reshape(wave_count, local_k, row_count)
    received = lax.all_to_all(payload, "wave", 0, 0, tiled=True)
    wave_table = make_table(owners, LON)
    received, wave_table = lax.optimization_barrier((received, wave_table))
    k_all = wave_count * local_k
    fourier = jnp.transpose(received.reshape(wave_count, 2, slot_count, row_count), (1, 0, 2, 3))
    fourier = fourier.reshape(k_all, lev_count, 2 * lat_count * 2)
    fourier = with_halo(fourier, (("lev", 1),), 1).reshape(k_all, -1)
    grid_vals = lax.dot_general(
        fourier, wave_table, (((0,), (0,)), ((), ())), preferred_element_type=jnp.float32
    ).reshape(lev_count + 2, 2, lat_count, 2, LON)
    centre = grid_vals[1:-1]
    slopes = 0.5 * (grid_vals[2:] - grid_vals[:-2])
    lead_t = centre[:, :, :, 0] * slopes[:, :, :, 1]
    second_t = centre[:, :, :, 1] * slopes[:, :, :, 0] + 0.5 * centre[:, :, :, 0] * centre[:, :, :, 1]
    tendency = jnp.stack([lead_t, second_t], axis=3).astype(jnp.bfloat16).reshape(row_count, LON)
    north = wave_index * lat_count + jnp.arange(lat_count, dtype=jnp.int32)
    latitude = jnp.stack([north, NLAT - 1 - north], axis=0)
    weight = jnp.sin((latitude.astype(jnp.float32) + 0.5) * (math.pi / NLAT)) / math.sqrt(NLAT)
    weight = jnp.broadcast_to(weight[None, :, :, None], (lev_count, 2, lat_count, 2)).reshape(-1)
    coeffs = lax.dot_general(
        wave_table, tendency, (((1,), (1,)), ((), ())), preferred_element_type=jnp.float32
    )
    coeffs = (coeffs * weight[None, :]).astype(jnp.bfloat16)
    coeffs = jnp.transpose(coeffs.reshape(2, wave_count, slot_count, row_count), (1, 0, 2, 3))
    owned = lax.all_to_all(coeffs.reshape(wave_count, local_k, row_count), "wave", 0, 0, tiled=True)
    owned = owned.reshape(wave_count, 2, pair_count, 2, lev_count, 2, lat_count, 2)
    owned = jnp.transpose(owned, (2, 4, 7, 1, 3, 5, 0, 6)).reshape(
        pair_count, lev_count, 2, 2, 2, 2, NLATH
    )
    partial = jnp.einsum(
        "plfrqhj,pjk->lfrpqhk", owned, legendre, preferred_element_type=jnp.float32
    )
    tendency_sum = in_first * (
        partial[:, :, :, :, 0, 0] + sign_first * partial[:, :, :, :, 0, 1]
    ) + in_second * (partial[:, :, :, :, 1, 0] + sign_second * partial[:, :, :, :, 1, 1])
    return tendency_sum.reshape(lev_count, 4, pair_count, NPK)


def solution(mesh):
    in_specs = (P("lev", None, "wave", None), P("wave", None, None), P())
    out_specs = P("lev", None, "wave", None)
    return jax.shard_map(shards, mesh=mesh, in_specs=in_specs, out_specs=out_specs, check_vma=False)
```

```python
import math

import jax
import jax.numpy as jnp
from jax import lax
from jax.experimental import pallas as pl
from jax.sharding import PartitionSpec as P

M = 640
NLAT = 1280
LON = 2688
NLATH = 640
NPK = 768


def with_halo(block, sides, width):
    for axis, dim in sides:
        count = lax.axis_size(axis)
        forward = [(i, i + 1) for i in range(count - 1)]
        backward = [(target, source) for source, target in forward]
        low = lax.ppermute(
            lax.slice_in_dim(block, block.shape[dim] - width, None, axis=dim), axis, forward
        )
        high = lax.ppermute(lax.slice_in_dim(block, 0, width, axis=dim), axis, backward)
        block = jnp.concatenate([low, block, high], axis=dim)
    return block


def dense_halo(block, axis, dim):
    count = lax.axis_size(axis)
    forward = [(i, i + 1) for i in range(count - 1)]
    backward = [(target, source) for source, target in forward]
    lead = block.shape[0]

    def send(part, pairs):
        shape = part.shape
        flat = part.reshape(-1, 128) if part.size % 128 == 0 else part.reshape(lead, -1)
        return lax.ppermute(flat, axis, pairs).reshape(shape)

    low = send(lax.slice_in_dim(block, block.shape[dim] - 1, None, axis=dim), forward)
    high = send(lax.slice_in_dim(block, 0, 1, axis=dim), backward)
    return jnp.concatenate([low, block, high], axis=dim)


def pair_masks(leading):
    packed = jnp.arange(NPK, dtype=jnp.int32)[None, :]
    split_at = (M - leading)[:, None]
    in_first = (packed < split_at).astype(jnp.float32)
    in_second = ((packed >= split_at) & (packed < M + 1)).astype(jnp.float32)
    sign_first = (1 - 2 * (packed % 2)).astype(jnp.float32)
    sign_second = (1 - 2 * ((packed - split_at) % 2)).astype(jnp.float32)
    return (in_first, in_second, sign_first, sign_second)


def table_kernel(cos_c_ref, sin_c_ref, cos_f_ref, sin_f_ref, out_ref):
    inner = cos_f_ref.shape[1]
    cos_f = cos_f_ref[...]
    sin_f = sin_f_ref[...]
    for k in range(cos_c_ref.shape[1]):
        cos_c = cos_c_ref[:, k : k + 1]
        sin_c = sin_c_ref[:, k : k + 1]
        columns = slice(k * inner, (k + 1) * inner)
        out_ref[0, :, columns] = (cos_c * cos_f - sin_c * sin_f).astype(out_ref.dtype)
        out_ref[1, :, columns] = (-(sin_c * cos_f + cos_c * sin_f)).astype(out_ref.dtype)


def make_table(owners, lon_count):
    inner = 128 if lon_count % 128 == 0 else lon_count
    outer = lon_count // inner
    scale = 2.0 * math.pi / lon_count
    fine = jnp.arange(inner, dtype=jnp.int32)
    coarse = jnp.arange(outer, dtype=jnp.int32) * inner
    fine_angle = (owners[:, None] * fine[None, :] % lon_count).astype(jnp.float32) * scale
    coarse_angle = (owners[:, None] * coarse[None, :] % lon_count).astype(jnp.float32) * scale
    rows = owners.shape[0]
    block = 128 if rows % 128 == 0 else rows
    table = pl.pallas_call(
        table_kernel,
        grid=(rows // block,),
        in_specs=[
            pl.BlockSpec((block, outer), lambda i: (i, 0)),
            pl.BlockSpec((block, outer), lambda i: (i, 0)),
            pl.BlockSpec((block, inner), lambda i: (i, 0)),
            pl.BlockSpec((block, inner), lambda i: (i, 0)),
        ],
        out_specs=pl.BlockSpec((2, block, lon_count), lambda i: (0, i, 0)),
        out_shape=jax.ShapeDtypeStruct((2, rows, lon_count), jnp.bfloat16),
    )(jnp.cos(coarse_angle), jnp.sin(coarse_angle), jnp.cos(fine_angle), jnp.sin(fine_angle))
    return table.reshape(2 * rows, lon_count)


def shards(spectrum, legendre, owners):
    lev_count = spectrum.shape[0]
    pair_count = spectrum.shape[2]
    slot_count = 2 * pair_count
    wave_count = lax.axis_size("wave")
    lat_count = NLATH // wave_count
    wave_index = lax.axis_index("wave")
    pair_base = wave_index * pair_count
    leading = lax.dynamic_slice_in_dim(owners[0::2], pair_base, pair_count)
    in_first, in_second, sign_first, sign_second = pair_masks(leading)
    mask_first = in_first.astype(jnp.bfloat16)
    mask_second = in_second.astype(jnp.bfloat16)
    signed_first = (in_first * sign_first).astype(jnp.bfloat16)
    signed_second = (in_second * sign_second).astype(jnp.bfloat16)
    spec_rows = spectrum.reshape(lev_count * 4, pair_count, NPK)
    masked = jnp.stack(
        [
            spec_rows * mask_first,
            spec_rows * mask_second,
            spec_rows * signed_first,
            spec_rows * signed_second,
        ],
        axis=2,
    ).reshape(lev_count, 2, 2, pair_count, 2, 2, NPK)
    waves = jnp.einsum(
        "lfrphqk,pjk->jrpqlhf", masked, legendre, preferred_element_type=jnp.float32
    ).astype(jnp.bfloat16)
    waves = waves.reshape(wave_count, lat_count, 2, pair_count, 2, lev_count, 2, 2)
    payload = jnp.transpose(waves, (0, 2, 3, 4, 5, 6, 1, 7))
    local_k = 2 * slot_count
    row_count = lev_count * 2 * lat_count * 2
    payload = payload.reshape(wave_count, local_k, row_count)
    received = lax.all_to_all(payload, "wave", 0, 0, tiled=True)
    wave_table = make_table(owners, LON)
    received, wave_table = lax.optimization_barrier((received, wave_table))
    k_all = wave_count * local_k
    level_rows = 2 * lat_count * 2
    fourier = dense_halo(received.reshape(wave_count, local_k, lev_count, level_rows), "lev", 2)
    fourier = jnp.transpose(
        fourier.reshape(wave_count, 2, slot_count, (lev_count + 2) * level_rows), (1, 0, 2, 3)
    ).reshape(k_all, -1)
    grid_vals = lax.dot_general(
        fourier, wave_table, (((0,), (0,)), ((), ())), preferred_element_type=jnp.float32
    ).reshape(lev_count + 2, 2, lat_count, 2, LON)
    centre = grid_vals[1:-1]
    slopes = 0.5 * (grid_vals[2:] - grid_vals[:-2])
    lead_t = centre[:, :, :, 0] * slopes[:, :, :, 1]
    second_t = centre[:, :, :, 1] * slopes[:, :, :, 0] + 0.5 * centre[:, :, :, 0] * centre[:, :, :, 1]
    tendency = jnp.stack([lead_t, second_t], axis=3).astype(jnp.bfloat16).reshape(row_count, LON)
    north = wave_index * lat_count + jnp.arange(lat_count, dtype=jnp.int32)
    latitude = jnp.stack([north, NLAT - 1 - north], axis=0)
    weight = jnp.sin((latitude.astype(jnp.float32) + 0.5) * (math.pi / NLAT)) / math.sqrt(NLAT)
    weight = jnp.broadcast_to(weight[None, :, :, None], (lev_count, 2, lat_count, 2)).reshape(-1)
    coeffs = lax.dot_general(
        wave_table, tendency, (((1,), (1,)), ((), ())), preferred_element_type=jnp.float32
    )
    coeffs = (coeffs * weight[None, :]).astype(jnp.bfloat16)
    coeffs = jnp.transpose(coeffs.reshape(2, wave_count, slot_count, row_count), (1, 0, 2, 3))
    owned = lax.all_to_all(coeffs.reshape(wave_count, local_k, row_count), "wave", 0, 0, tiled=True)
    owned = owned.reshape(wave_count, 2, pair_count, 2, lev_count, 2, lat_count, 2)
    owned = jnp.transpose(owned, (2, 4, 7, 1, 3, 5, 0, 6)).reshape(
        pair_count, lev_count, 2, 2, 2, 2, NLATH
    )
    partial = jnp.einsum(
        "plfrqhj,pjk->lfrpqhk", owned, legendre, preferred_element_type=jnp.float32
    )
    tendency_sum = in_first * (
        partial[:, :, :, :, 0, 0] + sign_first * partial[:, :, :, :, 0, 1]
    ) + in_second * (partial[:, :, :, :, 1, 0] + sign_second * partial[:, :, :, :, 1, 1])
    return tendency_sum.reshape(lev_count, 4, pair_count, NPK)


def solution(mesh):
    in_specs = (P("lev", None, "wave", None), P("wave", None, None), P())
    out_specs = P("lev", None, "wave", None)
    return jax.shard_map(shards, mesh=mesh, in_specs=in_specs, out_specs=out_specs, check_vma=False)
```

```python
import math

import jax
import jax.numpy as jnp
from jax import lax
from jax.experimental import pallas as pl
from jax.sharding import PartitionSpec as P

M = 640
NLAT = 1280
LON = 2688
NLATH = 640
NPK = 768


def with_halo(block, sides, width):
    for axis, dim in sides:
        count = lax.axis_size(axis)
        forward = [(i, i + 1) for i in range(count - 1)]
        backward = [(target, source) for source, target in forward]
        low = lax.ppermute(
            lax.slice_in_dim(block, block.shape[dim] - width, None, axis=dim), axis, forward
        )
        high = lax.ppermute(lax.slice_in_dim(block, 0, width, axis=dim), axis, backward)
        block = jnp.concatenate([low, block, high], axis=dim)
    return block


def dense_halo(block, axis, dim):
    count = lax.axis_size(axis)
    forward = [(i, i + 1) for i in range(count - 1)]
    backward = [(target, source) for source, target in forward]
    lead = block.shape[0]

    def send(part, pairs):
        shape = part.shape
        flat = part.reshape(-1, 128) if part.size % 128 == 0 else part.reshape(lead, -1)
        return lax.ppermute(flat, axis, pairs).reshape(shape)

    low = send(lax.slice_in_dim(block, block.shape[dim] - 1, None, axis=dim), forward)
    high = send(lax.slice_in_dim(block, 0, 1, axis=dim), backward)
    return jnp.concatenate([low, block, high], axis=dim)


def pair_masks(leading):
    packed = jnp.arange(NPK, dtype=jnp.int32)[None, :]
    split_at = (M - leading)[:, None]
    in_first = (packed < split_at).astype(jnp.float32)
    in_second = ((packed >= split_at) & (packed < M + 1)).astype(jnp.float32)
    sign_first = (1 - 2 * (packed % 2)).astype(jnp.float32)
    sign_second = (1 - 2 * ((packed - split_at) % 2)).astype(jnp.float32)
    return (in_first, in_second, sign_first, sign_second)


def table_kernel(cos_c_ref, sin_c_ref, cos_f_ref, sin_f_ref, out_ref):
    inner = cos_f_ref.shape[1]
    cos_f = cos_f_ref[...]
    sin_f = sin_f_ref[...]
    for k in range(cos_c_ref.shape[1]):
        cos_c = cos_c_ref[:, k : k + 1]
        sin_c = sin_c_ref[:, k : k + 1]
        columns = slice(k * inner, (k + 1) * inner)
        out_ref[0, :, columns] = (cos_c * cos_f - sin_c * sin_f).astype(out_ref.dtype)
        out_ref[1, :, columns] = (-(sin_c * cos_f + cos_c * sin_f)).astype(out_ref.dtype)


def make_table(owners, lon_count):
    inner = 128 if lon_count % 128 == 0 else lon_count
    outer = lon_count // inner
    scale = 2.0 * math.pi / lon_count
    fine = jnp.arange(inner, dtype=jnp.int32)
    coarse = jnp.arange(outer, dtype=jnp.int32) * inner
    fine_angle = (owners[:, None] * fine[None, :] % lon_count).astype(jnp.float32) * scale
    coarse_angle = (owners[:, None] * coarse[None, :] % lon_count).astype(jnp.float32) * scale
    rows = owners.shape[0]
    block = 128 if rows % 128 == 0 else rows
    table = pl.pallas_call(
        table_kernel,
        grid=(rows // block,),
        in_specs=[
            pl.BlockSpec((block, outer), lambda i: (i, 0)),
            pl.BlockSpec((block, outer), lambda i: (i, 0)),
            pl.BlockSpec((block, inner), lambda i: (i, 0)),
            pl.BlockSpec((block, inner), lambda i: (i, 0)),
        ],
        out_specs=pl.BlockSpec((2, block, lon_count), lambda i: (0, i, 0)),
        out_shape=jax.ShapeDtypeStruct((2, rows, lon_count), jnp.bfloat16),
    )(jnp.cos(coarse_angle), jnp.sin(coarse_angle), jnp.cos(fine_angle), jnp.sin(fine_angle))
    return table.reshape(2 * rows, lon_count)


def shards(spectrum, legendre, owners):
    lev_count = spectrum.shape[0]
    pair_count = spectrum.shape[2]
    slot_count = 2 * pair_count
    wave_count = lax.axis_size("wave")
    lat_count = NLATH // wave_count
    wave_index = lax.axis_index("wave")
    pair_base = wave_index * pair_count
    leading = lax.dynamic_slice_in_dim(owners[0::2], pair_base, pair_count)
    in_first, in_second, sign_first, sign_second = pair_masks(leading)
    mask_first = in_first.astype(jnp.bfloat16)
    mask_second = in_second.astype(jnp.bfloat16)
    signed_first = (in_first * sign_first).astype(jnp.bfloat16)
    signed_second = (in_second * sign_second).astype(jnp.bfloat16)
    spec_rows = dense_halo(spectrum, "lev", 0).reshape((lev_count + 2) * 4, pair_count, NPK)
    masked = jnp.stack(
        [
            spec_rows * mask_first,
            spec_rows * mask_second,
            spec_rows * signed_first,
            spec_rows * signed_second,
        ],
        axis=2,
    ).reshape(lev_count + 2, 2, 2, pair_count, 2, 2, NPK)
    waves = jnp.einsum(
        "lfrphqk,pjk->jrpqlhf", masked, legendre, preferred_element_type=jnp.float32
    ).astype(jnp.bfloat16)
    waves = waves.reshape(wave_count, lat_count, 2, pair_count, 2, lev_count + 2, 2, 2)
    payload = jnp.transpose(waves, (0, 2, 3, 4, 5, 6, 1, 7))
    local_k = 2 * slot_count
    row_count = lev_count * 2 * lat_count * 2
    payload = payload.reshape(wave_count, local_k, -1)
    received = lax.all_to_all(payload, "wave", 0, 0, tiled=True)
    wave_table = make_table(owners, LON)
    received, wave_table = lax.optimization_barrier((received, wave_table))
    k_all = wave_count * local_k
    fourier = jnp.transpose(
        received.reshape(wave_count, 2, slot_count, -1), (1, 0, 2, 3)
    ).reshape(k_all, -1)
    grid_vals = lax.dot_general(
        fourier, wave_table, (((0,), (0,)), ((), ())), preferred_element_type=jnp.float32
    ).reshape(lev_count + 2, 2, lat_count, 2, LON)
    centre = grid_vals[1:-1]
    slopes = 0.5 * (grid_vals[2:] - grid_vals[:-2])
    lead_t = centre[:, :, :, 0] * slopes[:, :, :, 1]
    second_t = centre[:, :, :, 1] * slopes[:, :, :, 0] + 0.5 * centre[:, :, :, 0] * centre[:, :, :, 1]
    tendency = jnp.stack([lead_t, second_t], axis=3).astype(jnp.bfloat16).reshape(row_count, LON)
    north = wave_index * lat_count + jnp.arange(lat_count, dtype=jnp.int32)
    latitude = jnp.stack([north, NLAT - 1 - north], axis=0)
    weight = jnp.sin((latitude.astype(jnp.float32) + 0.5) * (math.pi / NLAT)) / math.sqrt(NLAT)
    weight = jnp.broadcast_to(weight[None, :, :, None], (lev_count, 2, lat_count, 2)).reshape(-1)
    coeffs = lax.dot_general(
        wave_table, tendency, (((1,), (1,)), ((), ())), preferred_element_type=jnp.float32
    )
    coeffs = (coeffs * weight[None, :]).astype(jnp.bfloat16)
    coeffs = jnp.transpose(coeffs.reshape(2, wave_count, slot_count, row_count), (1, 0, 2, 3))
    owned = lax.all_to_all(coeffs.reshape(wave_count, local_k, row_count), "wave", 0, 0, tiled=True)
    owned = owned.reshape(wave_count, 2, pair_count, 2, lev_count, 2, lat_count, 2)
    owned = jnp.transpose(owned, (2, 4, 7, 1, 3, 5, 0, 6)).reshape(
        pair_count, lev_count, 2, 2, 2, 2, NLATH
    )
    partial = jnp.einsum(
        "plfrqhj,pjk->lfrpqhk", owned, legendre, preferred_element_type=jnp.float32
    )
    tendency_sum = in_first * (
        partial[:, :, :, :, 0, 0] + sign_first * partial[:, :, :, :, 0, 1]
    ) + in_second * (partial[:, :, :, :, 1, 0] + sign_second * partial[:, :, :, :, 1, 1])
    return tendency_sum.reshape(lev_count, 4, pair_count, NPK)


def solution(mesh):
    in_specs = (P("lev", None, "wave", None), P("wave", None, None), P())
    out_specs = P("lev", None, "wave", None)
    return jax.shard_map(shards, mesh=mesh, in_specs=in_specs, out_specs=out_specs, check_vma=False)
```

```python
import math

import jax
import jax.numpy as jnp
from jax import lax
from jax.experimental import pallas as pl
from jax.sharding import PartitionSpec as P

M = 640
NLAT = 1280
LON = 2688
NLATH = 640
NPK = 768


def with_halo(block, sides, width):
    for axis, dim in sides:
        count = lax.axis_size(axis)
        forward = [(i, i + 1) for i in range(count - 1)]
        backward = [(target, source) for source, target in forward]
        low = lax.ppermute(
            lax.slice_in_dim(block, block.shape[dim] - width, None, axis=dim), axis, forward
        )
        high = lax.ppermute(lax.slice_in_dim(block, 0, width, axis=dim), axis, backward)
        block = jnp.concatenate([low, block, high], axis=dim)
    return block


def dense_halo(block, axis, dim):
    count = lax.axis_size(axis)
    forward = [(i, i + 1) for i in range(count - 1)]
    backward = [(target, source) for source, target in forward]
    lead = block.shape[0]

    def send(part, pairs):
        shape = part.shape
        flat = part.reshape(-1, 128) if part.size % 128 == 0 else part.reshape(lead, -1)
        return lax.ppermute(flat, axis, pairs).reshape(shape)

    low = send(lax.slice_in_dim(block, block.shape[dim] - 1, None, axis=dim), forward)
    high = send(lax.slice_in_dim(block, 0, 1, axis=dim), backward)
    return jnp.concatenate([low, block, high], axis=dim)


def pair_masks(leading):
    packed = jnp.arange(NPK, dtype=jnp.int32)[None, :]
    split_at = (M - leading)[:, None]
    in_first = (packed < split_at).astype(jnp.float32)
    in_second = ((packed >= split_at) & (packed < M + 1)).astype(jnp.float32)
    sign_first = (1 - 2 * (packed % 2)).astype(jnp.float32)
    sign_second = (1 - 2 * ((packed - split_at) % 2)).astype(jnp.float32)
    return (in_first, in_second, sign_first, sign_second)


def table_kernel(cos_c_ref, sin_c_ref, cos_f_ref, sin_f_ref, out_ref):
    inner = cos_f_ref.shape[1]
    cos_f = cos_f_ref[...]
    sin_f = sin_f_ref[...]
    for k in range(cos_c_ref.shape[1]):
        cos_c = cos_c_ref[:, k : k + 1]
        sin_c = sin_c_ref[:, k : k + 1]
        columns = slice(k * inner, (k + 1) * inner)
        out_ref[0, :, columns] = (cos_c * cos_f - sin_c * sin_f).astype(out_ref.dtype)
        out_ref[1, :, columns] = (-(sin_c * cos_f + cos_c * sin_f)).astype(out_ref.dtype)


def make_table(owners, lon_count):
    inner = 128 if lon_count % 128 == 0 else lon_count
    outer = lon_count // inner
    scale = 2.0 * math.pi / lon_count
    fine = jnp.arange(inner, dtype=jnp.int32)
    coarse = jnp.arange(outer, dtype=jnp.int32) * inner
    fine_angle = (owners[:, None] * fine[None, :] % lon_count).astype(jnp.float32) * scale
    coarse_angle = (owners[:, None] * coarse[None, :] % lon_count).astype(jnp.float32) * scale
    rows = owners.shape[0]
    block = 128 if rows % 128 == 0 else rows
    table = pl.pallas_call(
        table_kernel,
        grid=(rows // block,),
        in_specs=[
            pl.BlockSpec((block, outer), lambda i: (i, 0)),
            pl.BlockSpec((block, outer), lambda i: (i, 0)),
            pl.BlockSpec((block, inner), lambda i: (i, 0)),
            pl.BlockSpec((block, inner), lambda i: (i, 0)),
        ],
        out_specs=pl.BlockSpec((2, block, lon_count), lambda i: (0, i, 0)),
        out_shape=jax.ShapeDtypeStruct((2, rows, lon_count), jnp.bfloat16),
    )(jnp.cos(coarse_angle), jnp.sin(coarse_angle), jnp.cos(fine_angle), jnp.sin(fine_angle))
    return table.reshape(2 * rows, lon_count)


def shards(spectrum, legendre, owners):
    lev_count = spectrum.shape[0]
    pair_count = spectrum.shape[2]
    slot_count = 2 * pair_count
    wave_count = lax.axis_size("wave")
    lat_count = NLATH // wave_count
    wave_index = lax.axis_index("wave")
    pair_base = wave_index * pair_count
    leading = lax.dynamic_slice_in_dim(owners[0::2], pair_base, pair_count)
    in_first, in_second, sign_first, sign_second = pair_masks(leading)
    mask_first = in_first.astype(jnp.bfloat16)
    mask_second = in_second.astype(jnp.bfloat16)
    signed_first = (in_first * sign_first).astype(jnp.bfloat16)
    signed_second = (in_second * sign_second).astype(jnp.bfloat16)
    spec_rows = dense_halo(spectrum, "lev", 0)
    wave_table = make_table(owners, LON)
    spec_rows, wave_table = lax.optimization_barrier((spec_rows, wave_table))
    spec_rows = spec_rows.reshape((lev_count + 2) * 4, pair_count, NPK)
    masked = jnp.stack(
        [
            spec_rows * mask_first,
            spec_rows * mask_second,
            spec_rows * signed_first,
            spec_rows * signed_second,
        ],
        axis=2,
    ).reshape(lev_count + 2, 2, 2, pair_count, 2, 2, NPK)
    waves = jnp.einsum(
        "lfrphqk,pjk->rpqlhfj", masked, legendre, preferred_element_type=jnp.float32
    ).astype(jnp.bfloat16)
    local_k = 2 * slot_count
    row_count = lev_count * 2 * 2 * lat_count
    payload = jnp.transpose(waves.reshape(-1, wave_count), (1, 0)).reshape(wave_count, local_k, -1)
    received = lax.all_to_all(payload, "wave", 0, 0, tiled=True)
    k_all = wave_count * local_k
    fourier = jnp.transpose(
        received.reshape(wave_count, 2, slot_count, -1), (1, 0, 2, 3)
    ).reshape(k_all, -1)
    grid_vals = lax.dot_general(
        fourier, wave_table, (((0,), (0,)), ((), ())), preferred_element_type=jnp.float32
    ).reshape(lev_count + 2, 2, 2, lat_count, LON)
    centre = grid_vals[1:-1]
    slopes = 0.5 * (grid_vals[2:] - grid_vals[:-2])
    lead_t = centre[:, :, 0] * slopes[:, :, 1]
    second_t = centre[:, :, 1] * slopes[:, :, 0] + 0.5 * centre[:, :, 0] * centre[:, :, 1]
    tendency = jnp.stack([lead_t, second_t], axis=2).astype(jnp.bfloat16).reshape(row_count, LON)
    north = jnp.arange(lat_count, dtype=jnp.int32) * wave_count + wave_index
    latitude = jnp.stack([north, NLAT - 1 - north], axis=0)
    weight = jnp.sin((latitude.astype(jnp.float32) + 0.5) * (math.pi / NLAT)) / math.sqrt(NLAT)
    weight = jnp.broadcast_to(weight[None, :, None, :], (lev_count, 2, 2, lat_count)).reshape(-1)
    coeffs = lax.dot_general(
        wave_table, tendency, (((1,), (1,)), ((), ())), preferred_element_type=jnp.float32
    )
    coeffs = (coeffs * weight[None, :]).astype(jnp.bfloat16)
    coeffs = jnp.transpose(coeffs.reshape(2, wave_count, slot_count, row_count), (1, 0, 2, 3))
    owned = lax.all_to_all(coeffs.reshape(wave_count, local_k, row_count), "wave", 0, 0, tiled=True)
    owned = jnp.transpose(owned.reshape(wave_count, -1), (1, 0)).reshape(
        2, pair_count, 2, lev_count, 2, 2, NLATH
    )
    owned = jnp.transpose(owned, (1, 3, 5, 0, 2, 4, 6))
    partial = jnp.einsum(
        "plfrqhj,pjk->lfrpqhk", owned, legendre, preferred_element_type=jnp.float32
    )
    tendency_sum = in_first * (
        partial[:, :, :, :, 0, 0] + sign_first * partial[:, :, :, :, 0, 1]
    ) + in_second * (partial[:, :, :, :, 1, 0] + sign_second * partial[:, :, :, :, 1, 1])
    return tendency_sum.reshape(lev_count, 4, pair_count, NPK)


def solution(mesh):
    in_specs = (P("lev", None, "wave", None), P("wave", None, None), P())
    out_specs = P("lev", None, "wave", None)
    return jax.shard_map(shards, mesh=mesh, in_specs=in_specs, out_specs=out_specs, check_vma=False)
```

```python
import math

import jax
import jax.numpy as jnp
from jax import lax
from jax.experimental import pallas as pl
from jax.sharding import PartitionSpec as P

M = 640
NLAT = 1280
LON = 2688
NLATH = 640
NPK = 768


def with_halo(block, sides, width):
    for axis, dim in sides:
        count = lax.axis_size(axis)
        forward = [(i, i + 1) for i in range(count - 1)]
        backward = [(target, source) for source, target in forward]
        low = lax.ppermute(
            lax.slice_in_dim(block, block.shape[dim] - width, None, axis=dim), axis, forward
        )
        high = lax.ppermute(lax.slice_in_dim(block, 0, width, axis=dim), axis, backward)
        block = jnp.concatenate([low, block, high], axis=dim)
    return block


def dense_halo(block, axis, dim):
    count = lax.axis_size(axis)
    forward = [(i, i + 1) for i in range(count - 1)]
    backward = [(target, source) for source, target in forward]
    lead = block.shape[0]

    def send(part, pairs):
        shape = part.shape
        flat = part.reshape(-1, 128) if part.size % 128 == 0 else part.reshape(lead, -1)
        return lax.ppermute(flat, axis, pairs).reshape(shape)

    low = send(lax.slice_in_dim(block, block.shape[dim] - 1, None, axis=dim), forward)
    high = send(lax.slice_in_dim(block, 0, 1, axis=dim), backward)
    return jnp.concatenate([low, block, high], axis=dim)


def pair_masks(leading):
    packed = jnp.arange(NPK, dtype=jnp.int32)[None, :]
    split_at = (M - leading)[:, None]
    in_first = (packed < split_at).astype(jnp.float32)
    in_second = ((packed >= split_at) & (packed < M + 1)).astype(jnp.float32)
    sign_first = (1 - 2 * (packed % 2)).astype(jnp.float32)
    sign_second = (1 - 2 * ((packed - split_at) % 2)).astype(jnp.float32)
    return (in_first, in_second, sign_first, sign_second)


def table_kernel(cos_c_ref, sin_c_ref, cos_f_ref, sin_f_ref, out_ref):
    inner = cos_f_ref.shape[1]
    cos_f = cos_f_ref[...]
    sin_f = sin_f_ref[...]
    for k in range(cos_c_ref.shape[1]):
        cos_c = cos_c_ref[:, k : k + 1]
        sin_c = sin_c_ref[:, k : k + 1]
        columns = slice(k * inner, (k + 1) * inner)
        out_ref[0, :, columns] = (cos_c * cos_f - sin_c * sin_f).astype(out_ref.dtype)
        out_ref[1, :, columns] = (-(sin_c * cos_f + cos_c * sin_f)).astype(out_ref.dtype)


def table_parts(owners, lon_count):
    inner = 128 if lon_count % 128 == 0 else lon_count
    outer = lon_count // inner
    scale = 2.0 * math.pi / lon_count
    fine = jnp.arange(inner, dtype=jnp.int32)
    coarse = jnp.arange(outer, dtype=jnp.int32) * inner
    fine_angle = (owners[:, None] * fine[None, :] % lon_count).astype(jnp.float32) * scale
    coarse_angle = (owners[:, None] * coarse[None, :] % lon_count).astype(jnp.float32) * scale
    return (jnp.cos(coarse_angle), jnp.sin(coarse_angle), jnp.cos(fine_angle), jnp.sin(fine_angle))


def make_table(parts, lon_count):
    rows, outer = parts[0].shape
    inner = parts[2].shape[1]
    block = 128 if rows % 128 == 0 else rows
    table = pl.pallas_call(
        table_kernel,
        grid=(rows // block,),
        in_specs=[
            pl.BlockSpec((block, outer), lambda i: (i, 0)),
            pl.BlockSpec((block, outer), lambda i: (i, 0)),
            pl.BlockSpec((block, inner), lambda i: (i, 0)),
            pl.BlockSpec((block, inner), lambda i: (i, 0)),
        ],
        out_specs=pl.BlockSpec((2, block, lon_count), lambda i: (0, i, 0)),
        out_shape=jax.ShapeDtypeStruct((2, rows, lon_count), jnp.bfloat16),
    )(*parts)
    return table.reshape(2 * rows, lon_count)


def shards(spectrum, legendre, owners):
    lev_count = spectrum.shape[0]
    pair_count = spectrum.shape[2]
    slot_count = 2 * pair_count
    wave_count = lax.axis_size("wave")
    lat_count = NLATH // wave_count
    wave_index = lax.axis_index("wave")
    pair_base = wave_index * pair_count
    leading = lax.dynamic_slice_in_dim(owners[0::2], pair_base, pair_count)
    in_first, in_second, sign_first, sign_second = pair_masks(leading)
    mask_first = in_first.astype(jnp.bfloat16)
    mask_second = in_second.astype(jnp.bfloat16)
    signed_first = (in_first * sign_first).astype(jnp.bfloat16)
    signed_second = (in_second * sign_second).astype(jnp.bfloat16)
    spec_rows = dense_halo(spectrum, "lev", 0)
    parts = table_parts(owners, LON)
    spec_rows, parts = lax.optimization_barrier((spec_rows, parts))
    spec_rows = spec_rows.reshape((lev_count + 2) * 4, pair_count, NPK)
    masked = jnp.stack(
        [
            spec_rows * mask_first,
            spec_rows * mask_second,
            spec_rows * signed_first,
            spec_rows * signed_second,
        ],
        axis=2,
    ).reshape(lev_count + 2, 2, 2, pair_count, 2, 2, NPK)
    waves = jnp.einsum(
        "lfrphqk,pjk->rpqlhfj", masked, legendre, preferred_element_type=jnp.float32
    ).astype(jnp.bfloat16)
    local_k = 2 * slot_count
    row_count = lev_count * 2 * 2 * lat_count
    payload = jnp.transpose(waves.reshape(-1, wave_count), (1, 0)).reshape(wave_count, local_k, -1)
    received = lax.all_to_all(payload, "wave", 0, 0, tiled=True)
    wave_table = make_table(parts, LON)
    received, wave_table = lax.optimization_barrier((received, wave_table))
    k_all = wave_count * local_k
    fourier = jnp.transpose(
        received.reshape(wave_count, 2, slot_count, -1), (1, 0, 2, 3)
    ).reshape(k_all, -1)
    grid_vals = lax.dot_general(
        fourier, wave_table, (((0,), (0,)), ((), ())), preferred_element_type=jnp.float32
    ).reshape(lev_count + 2, 2, 2, lat_count, LON)
    centre = grid_vals[1:-1]
    slopes = 0.5 * (grid_vals[2:] - grid_vals[:-2])
    lead_t = centre[:, :, 0] * slopes[:, :, 1]
    second_t = centre[:, :, 1] * slopes[:, :, 0] + 0.5 * centre[:, :, 0] * centre[:, :, 1]
    tendency = jnp.stack([lead_t, second_t], axis=2).astype(jnp.bfloat16).reshape(row_count, LON)
    north = jnp.arange(lat_count, dtype=jnp.int32) * wave_count + wave_index
    latitude = jnp.stack([north, NLAT - 1 - north], axis=0)
    weight = jnp.sin((latitude.astype(jnp.float32) + 0.5) * (math.pi / NLAT)) / math.sqrt(NLAT)
    weight = jnp.broadcast_to(weight[None, :, None, :], (lev_count, 2, 2, lat_count)).reshape(-1)
    coeffs = lax.dot_general(
        wave_table, tendency, (((1,), (1,)), ((), ())), preferred_element_type=jnp.float32
    )
    coeffs = (coeffs * weight[None, :]).astype(jnp.bfloat16)
    coeffs = jnp.transpose(coeffs.reshape(2, wave_count, slot_count, row_count), (1, 0, 2, 3))
    owned = lax.all_to_all(coeffs.reshape(wave_count, local_k, row_count), "wave", 0, 0, tiled=True)
    owned = jnp.transpose(owned.reshape(wave_count, -1), (1, 0)).reshape(
        2, pair_count, 2, lev_count, 2, 2, NLATH
    )
    owned = jnp.transpose(owned, (1, 3, 5, 0, 2, 4, 6))
    partial = jnp.einsum(
        "plfrqhj,pjk->lfrpqhk", owned, legendre, preferred_element_type=jnp.float32
    )
    tendency_sum = in_first * (
        partial[:, :, :, :, 0, 0] + sign_first * partial[:, :, :, :, 0, 1]
    ) + in_second * (partial[:, :, :, :, 1, 0] + sign_second * partial[:, :, :, :, 1, 1])
    return tendency_sum.reshape(lev_count, 4, pair_count, NPK)


def solution(mesh):
    in_specs = (P("lev", None, "wave", None), P("wave", None, None), P())
    out_specs = P("lev", None, "wave", None)
    return jax.shard_map(shards, mesh=mesh, in_specs=in_specs, out_specs=out_specs, check_vma=False)
```

```python
import math

import jax
import jax.numpy as jnp
from jax import lax
from jax.experimental import pallas as pl
from jax.sharding import PartitionSpec as P

M = 640
NLAT = 1280
LON = 2688
NLATH = 640
NPK = 768


def with_halo(block, sides, width):
    for axis, dim in sides:
        count = lax.axis_size(axis)
        forward = [(i, i + 1) for i in range(count - 1)]
        backward = [(target, source) for source, target in forward]
        low = lax.ppermute(
            lax.slice_in_dim(block, block.shape[dim] - width, None, axis=dim), axis, forward
        )
        high = lax.ppermute(lax.slice_in_dim(block, 0, width, axis=dim), axis, backward)
        block = jnp.concatenate([low, block, high], axis=dim)
    return block


def dense_halo(block, axis, dim):
    count = lax.axis_size(axis)
    forward = [(i, i + 1) for i in range(count - 1)]
    backward = [(target, source) for source, target in forward]
    lead = block.shape[0]

    def send(part, pairs):
        shape = part.shape
        flat = part.reshape(-1, 128) if part.size % 128 == 0 else part.reshape(lead, -1)
        return lax.ppermute(flat, axis, pairs).reshape(shape)

    low = send(lax.slice_in_dim(block, block.shape[dim] - 1, None, axis=dim), forward)
    high = send(lax.slice_in_dim(block, 0, 1, axis=dim), backward)
    return jnp.concatenate([low, block, high], axis=dim)


def pair_masks(leading):
    packed = jnp.arange(NPK, dtype=jnp.int32)[None, :]
    split_at = (M - leading)[:, None]
    in_first = (packed < split_at).astype(jnp.float32)
    in_second = ((packed >= split_at) & (packed < M + 1)).astype(jnp.float32)
    sign_first = (1 - 2 * (packed % 2)).astype(jnp.float32)
    sign_second = (1 - 2 * ((packed - split_at) % 2)).astype(jnp.float32)
    return (in_first, in_second, sign_first, sign_second)


def table_kernel(cos_c_ref, sin_c_ref, cos_f_ref, sin_f_ref, out_ref):
    inner = cos_f_ref.shape[1]
    cos_f = cos_f_ref[...]
    sin_f = sin_f_ref[...]
    for k in range(cos_c_ref.shape[1]):
        cos_c = cos_c_ref[:, k : k + 1]
        sin_c = sin_c_ref[:, k : k + 1]
        columns = slice(k * inner, (k + 1) * inner)
        out_ref[0, :, columns] = (cos_c * cos_f - sin_c * sin_f).astype(out_ref.dtype)
        out_ref[1, :, columns] = (-(sin_c * cos_f + cos_c * sin_f)).astype(out_ref.dtype)


def table_parts(owners, lon_count):
    inner = 128 if lon_count % 128 == 0 else lon_count
    outer = lon_count // inner
    scale = 2.0 * math.pi / lon_count
    fine = jnp.arange(inner, dtype=jnp.int32)
    coarse = jnp.arange(outer, dtype=jnp.int32) * inner
    fine_angle = (owners[:, None] * fine[None, :] % lon_count).astype(jnp.float32) * scale
    coarse_angle = (owners[:, None] * coarse[None, :] % lon_count).astype(jnp.float32) * scale
    return (jnp.cos(coarse_angle), jnp.sin(coarse_angle), jnp.cos(fine_angle), jnp.sin(fine_angle))


def make_table(parts, lon_count):
    rows, outer = parts[0].shape
    inner = parts[2].shape[1]
    block = 128 if rows % 128 == 0 else rows
    table = pl.pallas_call(
        table_kernel,
        grid=(rows // block,),
        in_specs=[
            pl.BlockSpec((block, outer), lambda i: (i, 0)),
            pl.BlockSpec((block, outer), lambda i: (i, 0)),
            pl.BlockSpec((block, inner), lambda i: (i, 0)),
            pl.BlockSpec((block, inner), lambda i: (i, 0)),
        ],
        out_specs=pl.BlockSpec((2, block, lon_count), lambda i: (0, i, 0)),
        out_shape=jax.ShapeDtypeStruct((2, rows, lon_count), jnp.bfloat16),
    )(*parts)
    return table.reshape(2 * rows, lon_count)


def shards(spectrum, legendre, owners):
    lev_count = spectrum.shape[0]
    pair_count = spectrum.shape[2]
    slot_count = 2 * pair_count
    wave_count = lax.axis_size("wave")
    lat_count = NLATH // wave_count
    wave_index = lax.axis_index("wave")
    pair_base = wave_index * pair_count
    leading = lax.dynamic_slice_in_dim(owners[0::2], pair_base, pair_count)
    in_first, in_second, sign_first, sign_second = pair_masks(leading)
    mask_first = in_first.astype(jnp.bfloat16)
    mask_second = in_second.astype(jnp.bfloat16)
    signed_first = (in_first * sign_first).astype(jnp.bfloat16)
    signed_second = (in_second * sign_second).astype(jnp.bfloat16)
    spec_rows = dense_halo(spectrum, "lev", 0)
    spec_rows = spec_rows.reshape((lev_count + 2) * 4, pair_count, NPK)
    masked = jnp.stack(
        [
            spec_rows * mask_first,
            spec_rows * mask_second,
            spec_rows * signed_first,
            spec_rows * signed_second,
        ],
        axis=2,
    ).reshape(lev_count + 2, 2, 2, pair_count, 2, 2, NPK)
    waves = jnp.einsum(
        "lfrphqk,pjk->rpqlhfj", masked, legendre, preferred_element_type=jnp.float32
    ).astype(jnp.bfloat16)
    local_k = 2 * slot_count
    row_count = lev_count * 2 * 2 * lat_count
    payload = jnp.transpose(waves.reshape(-1, wave_count), (1, 0)).reshape(wave_count, local_k, -1)
    received = lax.all_to_all(payload, "wave", 0, 0, tiled=True)
    wave_table = make_table(table_parts(owners, LON), LON)
    received, wave_table = lax.optimization_barrier((received, wave_table))
    k_all = wave_count * local_k
    fourier = jnp.transpose(
        received.reshape(wave_count, 2, slot_count, -1), (1, 0, 2, 3)
    ).reshape(k_all, -1)
    grid_vals = lax.dot_general(
        fourier, wave_table, (((0,), (0,)), ((), ())), preferred_element_type=jnp.float32
    ).reshape(lev_count + 2, 2, 2, lat_count, LON)
    centre = grid_vals[1:-1]
    slopes = 0.5 * (grid_vals[2:] - grid_vals[:-2])
    lead_t = centre[:, :, 0] * slopes[:, :, 1]
    second_t = centre[:, :, 1] * slopes[:, :, 0] + 0.5 * centre[:, :, 0] * centre[:, :, 1]
    tendency = jnp.stack([lead_t, second_t], axis=2).astype(jnp.bfloat16).reshape(row_count, LON)
    north = jnp.arange(lat_count, dtype=jnp.int32) * wave_count + wave_index
    latitude = jnp.stack([north, NLAT - 1 - north], axis=0)
    weight = jnp.sin((latitude.astype(jnp.float32) + 0.5) * (math.pi / NLAT)) / math.sqrt(NLAT)
    weight = jnp.broadcast_to(weight[None, :, None, :], (lev_count, 2, 2, lat_count)).reshape(-1)
    coeffs = lax.dot_general(
        wave_table, tendency, (((1,), (1,)), ((), ())), preferred_element_type=jnp.float32
    )
    coeffs = (coeffs * weight[None, :]).astype(jnp.bfloat16)
    coeffs = jnp.transpose(coeffs.reshape(2, wave_count, slot_count, row_count), (1, 0, 2, 3))
    owned = lax.all_to_all(coeffs.reshape(wave_count, local_k, row_count), "wave", 0, 0, tiled=True)
    owned = jnp.transpose(owned.reshape(wave_count, -1), (1, 0)).reshape(
        2, pair_count, 2, lev_count, 2, 2, NLATH
    )
    owned = jnp.transpose(owned, (1, 3, 5, 0, 2, 4, 6))
    partial = jnp.einsum(
        "plfrqhj,pjk->lfrpqhk", owned, legendre, preferred_element_type=jnp.float32
    )
    tendency_sum = in_first * (
        partial[:, :, :, :, 0, 0] + sign_first * partial[:, :, :, :, 0, 1]
    ) + in_second * (partial[:, :, :, :, 1, 0] + sign_second * partial[:, :, :, :, 1, 1])
    return tendency_sum.reshape(lev_count, 4, pair_count, NPK)


def solution(mesh):
    in_specs = (P("lev", None, "wave", None), P("wave", None, None), P())
    out_specs = P("lev", None, "wave", None)
    return jax.shard_map(shards, mesh=mesh, in_specs=in_specs, out_specs=out_specs, check_vma=False)
```

```python
import math

import jax
import jax.numpy as jnp
from jax import lax
from jax.experimental import pallas as pl
from jax.sharding import PartitionSpec as P

M = 640
NLAT = 1280
LON = 2688
NLATH = 640
NPK = 768


def with_halo(block, sides, width):
    for axis, dim in sides:
        count = lax.axis_size(axis)
        forward = [(i, i + 1) for i in range(count - 1)]
        backward = [(target, source) for source, target in forward]
        low = lax.ppermute(
            lax.slice_in_dim(block, block.shape[dim] - width, None, axis=dim), axis, forward
        )
        high = lax.ppermute(lax.slice_in_dim(block, 0, width, axis=dim), axis, backward)
        block = jnp.concatenate([low, block, high], axis=dim)
    return block


def dense_halo(block, axis, dim):
    count = lax.axis_size(axis)
    forward = [(i, i + 1) for i in range(count - 1)]
    backward = [(target, source) for source, target in forward]
    lead = block.shape[0]

    def send(part, pairs):
        shape = part.shape
        flat = part.reshape(-1, 128) if part.size % 128 == 0 else part.reshape(lead, -1)
        return lax.ppermute(flat, axis, pairs).reshape(shape)

    low = send(lax.slice_in_dim(block, block.shape[dim] - 1, None, axis=dim), forward)
    high = send(lax.slice_in_dim(block, 0, 1, axis=dim), backward)
    return jnp.concatenate([low, block, high], axis=dim)


def pair_masks(leading):
    packed = jnp.arange(NPK, dtype=jnp.int32)[None, :]
    split_at = (M - leading)[:, None]
    in_first = (packed < split_at).astype(jnp.float32)
    in_second = ((packed >= split_at) & (packed < M + 1)).astype(jnp.float32)
    sign_first = (1 - 2 * (packed % 2)).astype(jnp.float32)
    sign_second = (1 - 2 * ((packed - split_at) % 2)).astype(jnp.float32)
    return (in_first, in_second, sign_first, sign_second)


def table_kernel(cos_c_ref, sin_c_ref, cos_f_ref, sin_f_ref, out_ref):
    inner = cos_f_ref.shape[1]
    cos_f = cos_f_ref[...]
    sin_f = sin_f_ref[...]
    for k in range(cos_c_ref.shape[1]):
        cos_c = cos_c_ref[:, k : k + 1]
        sin_c = sin_c_ref[:, k : k + 1]
        columns = slice(k * inner, (k + 1) * inner)
        out_ref[0, :, columns] = (cos_c * cos_f - sin_c * sin_f).astype(out_ref.dtype)
        out_ref[1, :, columns] = (-(sin_c * cos_f + cos_c * sin_f)).astype(out_ref.dtype)


def table_parts(owners, lon_count):
    inner = 128 if lon_count % 128 == 0 else lon_count
    outer = lon_count // inner
    scale = 2.0 * math.pi / lon_count
    fine = jnp.arange(inner, dtype=jnp.int32)
    coarse = jnp.arange(outer, dtype=jnp.int32) * inner
    fine_angle = (owners[:, None] * fine[None, :] % lon_count).astype(jnp.float32) * scale
    coarse_angle = (owners[:, None] * coarse[None, :] % lon_count).astype(jnp.float32) * scale
    return (jnp.cos(coarse_angle), jnp.sin(coarse_angle), jnp.cos(fine_angle), jnp.sin(fine_angle))


def make_table(parts, lon_count):
    rows, outer = parts[0].shape
    inner = parts[2].shape[1]
    block = 128 if rows % 128 == 0 else rows
    table = pl.pallas_call(
        table_kernel,
        grid=(rows // block,),
        in_specs=[
            pl.BlockSpec((block, outer), lambda i: (i, 0)),
            pl.BlockSpec((block, outer), lambda i: (i, 0)),
            pl.BlockSpec((block, inner), lambda i: (i, 0)),
            pl.BlockSpec((block, inner), lambda i: (i, 0)),
        ],
        out_specs=pl.BlockSpec((2, block, lon_count), lambda i: (0, i, 0)),
        out_shape=jax.ShapeDtypeStruct((2, rows, lon_count), jnp.bfloat16),
    )(*parts)
    return table.reshape(2 * rows, lon_count)


def shards(spectrum, legendre, owners):
    lev_count = spectrum.shape[0]
    pair_count = spectrum.shape[2]
    slot_count = 2 * pair_count
    wave_count = lax.axis_size("wave")
    lat_count = NLATH // wave_count
    wave_index = lax.axis_index("wave")
    pair_base = wave_index * pair_count
    leading = lax.dynamic_slice_in_dim(owners[0::2], pair_base, pair_count)
    in_first, in_second, sign_first, sign_second = pair_masks(leading)
    mask_first = in_first.astype(jnp.bfloat16)
    mask_second = in_second.astype(jnp.bfloat16)
    signed_first = (in_first * sign_first).astype(jnp.bfloat16)
    signed_second = (in_second * sign_second).astype(jnp.bfloat16)
    lev_index = lax.axis_index("lev")
    every_level = lax.all_gather(spectrum, "lev", axis=0, tiled=True)
    zero_level = jnp.zeros((1,) + spectrum.shape[1:], spectrum.dtype)
    every_level = jnp.concatenate([zero_level, every_level, zero_level], axis=0)
    spec_rows = lax.dynamic_slice_in_dim(every_level, lev_index * lev_count, lev_count + 2, axis=0)
    spec_rows = spec_rows.reshape((lev_count + 2) * 4, pair_count, NPK)
    masked = jnp.stack(
        [
            spec_rows * mask_first,
            spec_rows * mask_second,
            spec_rows * signed_first,
            spec_rows * signed_second,
        ],
        axis=2,
    ).reshape(lev_count + 2, 2, 2, pair_count, 2, 2, NPK)
    waves = jnp.einsum(
        "lfrphqk,pjk->rpqlhfj", masked, legendre, preferred_element_type=jnp.float32
    ).astype(jnp.bfloat16)
    local_k = 2 * slot_count
    row_count = lev_count * 2 * 2 * lat_count
    payload = jnp.transpose(waves.reshape(-1, wave_count), (1, 0)).reshape(wave_count, local_k, -1)
    received = lax.all_to_all(payload, "wave", 0, 0, tiled=True)
    wave_table = make_table(table_parts(owners, LON), LON)
    received, wave_table = lax.optimization_barrier((received, wave_table))
    k_all = wave_count * local_k
    fourier = jnp.transpose(
        received.reshape(wave_count, 2, slot_count, -1), (1, 0, 2, 3)
    ).reshape(k_all, -1)
    grid_vals = lax.dot_general(
        fourier, wave_table, (((0,), (0,)), ((), ())), preferred_element_type=jnp.float32
    ).reshape(lev_count + 2, 2, 2, lat_count, LON)
    centre = grid_vals[1:-1]
    slopes = 0.5 * (grid_vals[2:] - grid_vals[:-2])
    lead_t = centre[:, :, 0] * slopes[:, :, 1]
    second_t = centre[:, :, 1] * slopes[:, :, 0] + 0.5 * centre[:, :, 0] * centre[:, :, 1]
    tendency = jnp.stack([lead_t, second_t], axis=2).astype(jnp.bfloat16).reshape(row_count, LON)
    north = jnp.arange(lat_count, dtype=jnp.int32) * wave_count + wave_index
    latitude = jnp.stack([north, NLAT - 1 - north], axis=0)
    weight = jnp.sin((latitude.astype(jnp.float32) + 0.5) * (math.pi / NLAT)) / math.sqrt(NLAT)
    weight = jnp.broadcast_to(weight[None, :, None, :], (lev_count, 2, 2, lat_count)).reshape(-1)
    coeffs = lax.dot_general(
        wave_table, tendency, (((1,), (1,)), ((), ())), preferred_element_type=jnp.float32
    )
    coeffs = (coeffs * weight[None, :]).astype(jnp.bfloat16)
    coeffs = jnp.transpose(coeffs.reshape(2, wave_count, slot_count, row_count), (1, 0, 2, 3))
    owned = lax.all_to_all(coeffs.reshape(wave_count, local_k, row_count), "wave", 0, 0, tiled=True)
    owned = jnp.transpose(owned.reshape(wave_count, -1), (1, 0)).reshape(
        2, pair_count, 2, lev_count, 2, 2, NLATH
    )
    owned = jnp.transpose(owned, (1, 3, 5, 0, 2, 4, 6))
    partial = jnp.einsum(
        "plfrqhj,pjk->lfrpqhk", owned, legendre, preferred_element_type=jnp.float32
    )
    tendency_sum = in_first * (
        partial[:, :, :, :, 0, 0] + sign_first * partial[:, :, :, :, 0, 1]
    ) + in_second * (partial[:, :, :, :, 1, 0] + sign_second * partial[:, :, :, :, 1, 1])
    return tendency_sum.reshape(lev_count, 4, pair_count, NPK)


def solution(mesh):
    in_specs = (P("lev", None, "wave", None), P("wave", None, None), P())
    out_specs = P("lev", None, "wave", None)
    return jax.shard_map(shards, mesh=mesh, in_specs=in_specs, out_specs=out_specs, check_vma=False)
```

```python
import math

import jax
import jax.numpy as jnp
from jax import lax
from jax.experimental import pallas as pl
from jax.sharding import PartitionSpec as P

M = 640
NLAT = 1280
LON = 2688
NLATH = 640
NPK = 768


def with_halo(block, sides, width):
    for axis, dim in sides:
        count = lax.axis_size(axis)
        forward = [(i, i + 1) for i in range(count - 1)]
        backward = [(target, source) for source, target in forward]
        low = lax.ppermute(
            lax.slice_in_dim(block, block.shape[dim] - width, None, axis=dim), axis, forward
        )
        high = lax.ppermute(lax.slice_in_dim(block, 0, width, axis=dim), axis, backward)
        block = jnp.concatenate([low, block, high], axis=dim)
    return block


def dense_halo(block, axis, dim):
    count = lax.axis_size(axis)
    forward = [(i, i + 1) for i in range(count - 1)]
    backward = [(target, source) for source, target in forward]
    lead = block.shape[0]

    def send(part, pairs):
        shape = part.shape
        flat = part.reshape(-1, 128) if part.size % 128 == 0 else part.reshape(lead, -1)
        return lax.ppermute(flat, axis, pairs).reshape(shape)

    low = send(lax.slice_in_dim(block, block.shape[dim] - 1, None, axis=dim), forward)
    high = send(lax.slice_in_dim(block, 0, 1, axis=dim), backward)
    return jnp.concatenate([low, block, high], axis=dim)


def pair_masks(leading):
    packed = jnp.arange(NPK, dtype=jnp.int32)[None, :]
    split_at = (M - leading)[:, None]
    in_first = (packed < split_at).astype(jnp.float32)
    in_second = ((packed >= split_at) & (packed < M + 1)).astype(jnp.float32)
    sign_first = (1 - 2 * (packed % 2)).astype(jnp.float32)
    sign_second = (1 - 2 * ((packed - split_at) % 2)).astype(jnp.float32)
    return (in_first, in_second, sign_first, sign_second)


def table_kernel(cos_c_ref, sin_c_ref, cos_f_ref, sin_f_ref, out_ref):
    inner = cos_f_ref.shape[1]
    cos_f = cos_f_ref[...]
    sin_f = sin_f_ref[...]
    for k in range(cos_c_ref.shape[1]):
        cos_c = cos_c_ref[:, k : k + 1]
        sin_c = sin_c_ref[:, k : k + 1]
        columns = slice(k * inner, (k + 1) * inner)
        out_ref[0, :, columns] = (cos_c * cos_f - sin_c * sin_f).astype(out_ref.dtype)
        out_ref[1, :, columns] = (-(sin_c * cos_f + cos_c * sin_f)).astype(out_ref.dtype)


def table_parts(owners, lon_count):
    inner = 128 if lon_count % 128 == 0 else lon_count
    outer = lon_count // inner
    scale = 2.0 * math.pi / lon_count
    fine = jnp.arange(inner, dtype=jnp.int32)
    coarse = jnp.arange(outer, dtype=jnp.int32) * inner
    fine_angle = (owners[:, None] * fine[None, :] % lon_count).astype(jnp.float32) * scale
    coarse_angle = (owners[:, None] * coarse[None, :] % lon_count).astype(jnp.float32) * scale
    return (jnp.cos(coarse_angle), jnp.sin(coarse_angle), jnp.cos(fine_angle), jnp.sin(fine_angle))


def make_table(parts, lon_count):
    rows, outer = parts[0].shape
    inner = parts[2].shape[1]
    block = 128 if rows % 128 == 0 else rows
    table = pl.pallas_call(
        table_kernel,
        grid=(rows // block,),
        in_specs=[
            pl.BlockSpec((block, outer), lambda i: (i, 0)),
            pl.BlockSpec((block, outer), lambda i: (i, 0)),
            pl.BlockSpec((block, inner), lambda i: (i, 0)),
            pl.BlockSpec((block, inner), lambda i: (i, 0)),
        ],
        out_specs=pl.BlockSpec((2, block, lon_count), lambda i: (0, i, 0)),
        out_shape=jax.ShapeDtypeStruct((2, rows, lon_count), jnp.bfloat16),
    )(*parts)
    return table.reshape(2 * rows, lon_count)


def shards(spectrum, legendre, owners):
    lev_count = spectrum.shape[0]
    pair_count = spectrum.shape[2]
    slot_count = 2 * pair_count
    wave_count = lax.axis_size("wave")
    lat_count = NLATH // wave_count
    wave_index = lax.axis_index("wave")
    pair_base = wave_index * pair_count
    leading = lax.dynamic_slice_in_dim(owners[0::2], pair_base, pair_count)
    in_first, in_second, sign_first, sign_second = pair_masks(leading)
    mask_first = in_first.astype(jnp.bfloat16)
    mask_second = in_second.astype(jnp.bfloat16)
    signed_first = (in_first * sign_first).astype(jnp.bfloat16)
    signed_second = (in_second * sign_second).astype(jnp.bfloat16)
    def waves_of(levels):
        rows = levels.reshape(levels.shape[0] * 4, pair_count, NPK)
        masked = jnp.stack(
            [rows * mask_first, rows * mask_second, rows * signed_first, rows * signed_second],
            axis=2,
        ).reshape(levels.shape[0], 2, 2, pair_count, 2, 2, NPK)
        return jnp.einsum(
            "lfrphqk,pjk->rpqlhfj", masked, legendre, preferred_element_type=jnp.float32
        ).astype(jnp.bfloat16)

    own = waves_of(spectrum)
    halo = dense_halo(spectrum, "lev", 0)
    near = waves_of(jnp.concatenate([halo[:1], halo[-1:]], axis=0))
    waves = jnp.concatenate([near[:, :, :, :1], own, near[:, :, :, 1:]], axis=3)
    local_k = 2 * slot_count
    row_count = lev_count * 2 * 2 * lat_count
    payload = jnp.transpose(waves.reshape(-1, wave_count), (1, 0)).reshape(wave_count, local_k, -1)
    received = lax.all_to_all(payload, "wave", 0, 0, tiled=True)
    wave_table = make_table(table_parts(owners, LON), LON)
    received, wave_table = lax.optimization_barrier((received, wave_table))
    k_all = wave_count * local_k
    fourier = jnp.transpose(
        received.reshape(wave_count, 2, slot_count, -1), (1, 0, 2, 3)
    ).reshape(k_all, -1)
    grid_vals = lax.dot_general(
        fourier, wave_table, (((0,), (0,)), ((), ())), preferred_element_type=jnp.float32
    ).reshape(lev_count + 2, 2, 2, lat_count, LON)
    centre = grid_vals[1:-1]
    slopes = 0.5 * (grid_vals[2:] - grid_vals[:-2])
    lead_t = centre[:, :, 0] * slopes[:, :, 1]
    second_t = centre[:, :, 1] * slopes[:, :, 0] + 0.5 * centre[:, :, 0] * centre[:, :, 1]
    tendency = jnp.stack([lead_t, second_t], axis=2).astype(jnp.bfloat16).reshape(row_count, LON)
    north = jnp.arange(lat_count, dtype=jnp.int32) * wave_count + wave_index
    latitude = jnp.stack([north, NLAT - 1 - north], axis=0)
    weight = jnp.sin((latitude.astype(jnp.float32) + 0.5) * (math.pi / NLAT)) / math.sqrt(NLAT)
    weight = jnp.broadcast_to(weight[None, :, None, :], (lev_count, 2, 2, lat_count)).reshape(-1)
    coeffs = lax.dot_general(
        wave_table, tendency, (((1,), (1,)), ((), ())), preferred_element_type=jnp.float32
    )
    coeffs = (coeffs * weight[None, :]).astype(jnp.bfloat16)
    coeffs = jnp.transpose(coeffs.reshape(2, wave_count, slot_count, row_count), (1, 0, 2, 3))
    owned = lax.all_to_all(coeffs.reshape(wave_count, local_k, row_count), "wave", 0, 0, tiled=True)
    owned = jnp.transpose(owned.reshape(wave_count, -1), (1, 0)).reshape(
        2, pair_count, 2, lev_count, 2, 2, NLATH
    )
    owned = jnp.transpose(owned, (1, 3, 5, 0, 2, 4, 6))
    partial = jnp.einsum(
        "plfrqhj,pjk->lfrpqhk", owned, legendre, preferred_element_type=jnp.float32
    )
    tendency_sum = in_first * (
        partial[:, :, :, :, 0, 0] + sign_first * partial[:, :, :, :, 0, 1]
    ) + in_second * (partial[:, :, :, :, 1, 0] + sign_second * partial[:, :, :, :, 1, 1])
    return tendency_sum.reshape(lev_count, 4, pair_count, NPK)


def solution(mesh):
    in_specs = (P("lev", None, "wave", None), P("wave", None, None), P())
    out_specs = P("lev", None, "wave", None)
    return jax.shard_map(shards, mesh=mesh, in_specs=in_specs, out_specs=out_specs, check_vma=False)
```
